512 devices in a mesh: seq: 32 (over x_lo, z, core), tensor: 16 (over x_hi, y).
Axes of the slice: x: 4 (x_hi: 2, x_lo: 2; x = x_hi * 2 + x_lo), y: 8, z: 8, core: 2. Of those that a mesh axis runs over, the one named last changes fastest.
Arguments:
- qkv: bfloat16 [3, 8192, 8192], P(None, 'seq', 'tensor'), may hold values from -6 to 6
- conv_weight: float32 [3, 3, 8192], P(None, None, 'tensor'), may hold values from -3.6 to 3.6
- decay_rate: float32 [16, 8192], P(None, 'tensor'), may hold values from 1e-05 to 0.06
- residue: float32 [16, 8192], P(None, 'tensor'), may hold values from -3 to 3
- skip_gain: float32 [8192], P('tensor'), may hold values from -5 to 5
- out_weight: bfloat16 [8192, 8192], P('seq', 'tensor'), may hold values from -0.125 to 0.125
Outputs:
- mixer_out: bfloat16 [8192, 8192], P('seq', 'tensor')
The draws below stay inside these ranges and needn't reach their ends.
All inputs are finite; a program needn't handle non-finite values.
Results may differ from the reference program's by a relative error of at most 0.0049.
Values may be sent and summed in bfloat16 or wider, within the bound.
No kernel may reach another device: no remote copies, remote signals or barrier semaphores. Data moves between devices by JAX's collectives and lax.ppermute only.
A program may use at most 64 MiB of HBM per device.

```python
import math
from functools import partial
import jax
import jax.numpy as jnp
from jax import lax

D = 8192
M = 16
KS = 3
TOK_DEV = 256
TOKENS = 8192


def draw_decay_rate(key, part):
    key_pick, key_slow, key_fast = jax.random.split(key, 3)
    share_slow = 0.5
    slow_top = 1.0 / TOKENS
    picked = jax.random.uniform(key_pick, (M, D), jnp.float32) < share_slow
    slow_values = jnp.exp(math.log(1e-05) + jax.random.uniform(key_slow, (M, D), jnp.float32) * (math.log(slow_top) - math.log(1e-05)))
    fast_values = jnp.exp(math.log(slow_top) + jax.random.uniform(key_fast, (M, D), jnp.float32) * (math.log(0.06) - math.log(slow_top)))
    return jnp.clip(jnp.where(picked, slow_values, fast_values), 1e-05, 0.06).astype(jnp.float32)


def raised(drawn, stream_key, source, target, parts, factor):
    def block_of(dim):
        return (jnp.arange(drawn.shape[dim]) // (drawn.shape[dim] // parts)).reshape((-1,) + (1,) * (drawn.ndim - 1 - dim))

    first = jax.random.permutation(stream_key, parts)[block_of(target)]
    second = (block_of(target) + parts // 2) % parts
    return jnp.where((block_of(source) == first) | (block_of(source) == second), factor * drawn, drawn)


def level_of(rng, dims, shards, low, top_value):
    gain, own = 1.0, jax.random.fold_in(rng, 6)
    for dim, shards_of in shards:
        heights = jnp.exp(jax.random.uniform(jax.random.fold_in(own, dim), (shards_of,), jnp.float32, low / len(shards), top_value / len(shards)))
        gain = gain * jnp.repeat(heights, dims[dim] // shards_of).reshape([-1 if axis == dim else 1 for axis in range(len(dims))])
    return gain


def normal_values(own_key, dims, scale, bound, cuts=(), kind=jnp.bfloat16):
    array = scale * jax.random.normal(own_key, dims, jnp.float32)
    if cuts:
        array = array * level_of(own_key, dims, cuts, -0.22, 0.18)
    return jnp.clip(array, -bound, bound).astype(kind)


def gaussian_with(own_key, extent, spread, bound, shards, heavy, kind=jnp.bfloat16):
    values = spread * jax.random.normal(own_key, extent, jnp.float32)
    if shards:
        values = values * level_of(own_key, extent, shards, -0.22, 0.18)
    return jnp.clip(raised(values, jax.random.fold_in(own_key, 3), *heavy), -bound, bound).astype(kind)


def setup_inputs(seed: int = 0) -> dict:
    splits = jax.random.split(jax.random.key(seed), 7)
    return {
        "qkv": normal_values(splits[0], (3, TOKENS, D), 1.0, 6.0, ((1, 32), (2, 16))),
        "conv_weight": normal_values(splits[1], (3, KS, D), 0.6, 3.6, ((2, 16),), jnp.float32),
        "decay_rate": draw_decay_rate(jax.random.fold_in(splits[6], 71), 0),
        "residue": normal_values(splits[3], (M, D), 0.5, 3.0, ((1, 16),), jnp.float32),
        "skip_gain": normal_values(splits[4], (D,), 1.0, 5.0, ((0, 16),), jnp.float32),
        "out_weight": gaussian_with(splits[5], (D, D), D ** -0.5, 0.125, ((0, 32), (1, 16)), (0, 1, 32, 2.75)),
    }


PRECISE = lax.Precision.HIGHEST

def short_filter(padded, conv_weight, length):
    result = jnp.zeros((padded.shape[0], length, padded.shape[2]), jnp.float32)
    for offset in range(KS):
        start_row = KS - 1 - offset
        result = result + conv_weight[:, offset, None, :] * padded[:, start_row:start_row + length, :]
    return result

def mode_tables(rate_block, residue_block, length):
    lag_values = jnp.arange(length, dtype=jnp.float32)
    decay_table = jnp.exp(-rate_block[:, None, :] * lag_values[None, :, None])
    mode_weight = residue_block * jnp.sqrt(-jnp.expm1(-2.0 * rate_block))
    return (decay_table, mode_weight)

def toeplitz(filter_taps):
    length = filter_taps.shape[0]
    lag_index = jnp.arange(length)[:, None] - jnp.arange(length)[None, :]
    picked = filter_taps[jnp.maximum(lag_index, 0), :]
    return jnp.where(lag_index[:, :, None] >= 0, picked, 0.0)

def modal_block(block_len, inputs):
    x_block, rate_block, residue_block = inputs
    decay_table, mode_weight = mode_tables(rate_block, residue_block, block_len)
    filter_taps = jnp.einsum('mc,mdc->dc', mode_weight, decay_table, precision=PRECISE)
    matrix = toeplitz(filter_taps)
    inner_part = jnp.einsum('tsc,nsc->ntc', matrix, x_block, precision=PRECISE)
    local_state = jnp.einsum('msc,nsc->nmc', decay_table[:, ::-1, :], x_block, precision=PRECISE)
    block_decay = jnp.exp(-rate_block * block_len)

    def advance(state, segment):
        return (state * block_decay + segment, state)
    _, entering = lax.scan(advance, jnp.zeros(rate_block.shape, jnp.float32), local_state)
    later_table = decay_table * jnp.exp(-rate_block)[:, None, :]
    carried = jnp.einsum('mc,mdc,nmc->ndc', mode_weight, later_table, entering, precision=PRECISE)
    return inner_part + carried

def reference(qkv, conv_weight, decay_rate, residue, skip_gain, out_weight):
    length = qkv.shape[1]
    features_in = qkv.astype(jnp.float32)
    padded = jnp.pad(features_in, ((0, 0), (KS - 1, 0), (0, 0)))
    filtered = short_filter(padded, conv_weight, length)
    product = filtered[1] * filtered[2]
    channels = product.shape[1]
    group_width = min(channels, 128)
    groups = channels // group_width
    block_len = min(TOK_DEV, 64)
    block_count = length // block_len
    x_groups = product.reshape(block_count, block_len, groups, group_width).transpose(2, 0, 1, 3)
    rate_groups = decay_rate.reshape(M, groups, group_width).transpose(1, 0, 2)
    residue_groups = residue.reshape(M, groups, group_width).transpose(1, 0, 2)
    long_groups = lax.map(partial(modal_block, block_len), (x_groups, rate_groups, residue_groups))
    long_part = long_groups.transpose(1, 2, 0, 3).reshape(length, channels)
    long_part = long_part + skip_gain[None, :] * product
    mixed = (filtered[0] * long_part).astype(jnp.bfloat16)
    return jnp.dot(mixed, out_weight, preferred_element_type=jnp.float32).astype(jnp.bfloat16)
```

```python
import jax
import jax.numpy as jnp
from jax import lax
from jax.sharding import PartitionSpec as P


KS = 3


PRECISE = lax.Precision.HIGHEST


def passed_along(block, axis, distance):
    devices = range(lax.axis_size(axis))
    route = [(i - distance, i) for i in devices if i - distance in devices]
    return lax.ppermute(block, axis, route)


def entering_state(local_state, rate, tokens_here, axis):
    sections = lax.axis_size(axis)
    decay = jnp.exp(-rate * tokens_here)
    state = passed_along(local_state, axis, 1)
    if sections > 2:
        state = state + decay * passed_along(local_state, axis, 2)
    distance = 2
    while distance < sections:
        state = state + jnp.exp(-rate * (tokens_here * distance)) * passed_along(state, axis, distance)
        distance *= 2
    return state


def body(qkv, conv_weight, decay_rate, residue, skip_gain, out_weight):
    tokens_here = qkv.shape[1]
    channels = qkv.shape[2]
    tail_rows = qkv[:, tokens_here - (KS - 1) :, :]
    previous = passed_along(tail_rows, "seq", 1)
    extended = jnp.concatenate([previous, qkv], axis=1).astype(jnp.float32)
    filtered = jnp.zeros((3, tokens_here, channels), jnp.float32)
    for offset in range(KS):
        start_row = KS - 1 - offset
        filtered = (
            filtered
            + conv_weight[:, offset, None, :] * extended[:, start_row : start_row + tokens_here, :]
        )
    product = filtered[1] * filtered[2]

    return finish(filtered, product, decay_rate, residue, skip_gain, out_weight)


def finish(filtered, product, decay_rate, residue, skip_gain, out_weight):
    tokens_here, channels = product.shape
    modes = decay_rate.shape[0]
    rate = decay_rate
    mode_weight = residue * jnp.sqrt(-jnp.expm1(-2.0 * rate))
    lags = jnp.arange(tokens_here, dtype=jnp.float32)[:, None, None]
    growth = jnp.exp(rate[None] * lags)
    scaled = (growth * product[:, None, :]).reshape(tokens_here, modes * channels)
    lower = (jnp.arange(tokens_here)[:, None] >= jnp.arange(tokens_here)[None, :]).astype(jnp.float32)
    running = jnp.dot(lower, scaled, precision=PRECISE).reshape(tokens_here, modes, channels)
    local_state = jnp.exp(-rate * (tokens_here - 1)) * running[tokens_here - 1]
    section_entering = entering_state(local_state, rate, tokens_here, "seq")
    shrink = jnp.exp(-rate[None] * lags)
    total = running + jnp.exp(-rate) * section_entering
    long_part = jnp.sum(mode_weight[None] * shrink * total, axis=1)
    long_part = long_part + skip_gain[None, :] * product
    mixed_local = (filtered[0] * long_part).astype(jnp.bfloat16)
    features = lax.all_gather(mixed_local, "tensor", axis=1, tiled=True)
    weight_all = lax.all_gather(out_weight, "seq", axis=0, tiled=True)
    projected = jnp.dot(
        features,
        weight_all,
        preferred_element_type=jnp.float32,
    )
    return projected.astype(jnp.bfloat16)


def solution(mesh):
    return jax.shard_map(
        body,
        mesh=mesh,
        in_specs=(
            P(None, "seq", "tensor"),
            P(None, None, "tensor"),
            P(None, "tensor"),
            P(None, "tensor"),
            P("tensor"),
            P("seq", "tensor"),
        ),
        out_specs=P("seq", "tensor"),
        check_vma=False,
    )
```

```python
import jax
import jax.numpy as jnp
from jax import lax
from jax.sharding import PartitionSpec as P


KS = 3


PRECISE = lax.Precision.HIGHEST


def passed_along(block, axis, distance):
    devices = range(lax.axis_size(axis))
    route = [(i - distance, i) for i in devices if i - distance in devices]
    return lax.ppermute(block, axis, route)


def entering_state(local_state, rate, tokens_here, axis):
    sections = lax.axis_size(axis)
    decay = jnp.exp(-rate * tokens_here)
    state = passed_along(local_state, axis, 1)
    if sections > 2:
        state = state + decay * passed_along(local_state, axis, 2)
    distance = 2
    while distance < sections:
        state = state + jnp.exp(-rate * (tokens_here * distance)) * passed_along(state, axis, distance)
        distance *= 2
    return state


def body(qkv, conv_weight, decay_rate, residue, skip_gain, out_weight):
    tokens_here = qkv.shape[1]
    channels = qkv.shape[2]
    tail_rows = qkv[:, tokens_here - (KS - 1) :, :]
    previous = passed_along(tail_rows, "seq", 1)
    extended = jnp.concatenate([previous, qkv], axis=1).astype(jnp.float32)
    filtered = jnp.zeros((3, tokens_here, channels), jnp.float32)
    for offset in range(KS):
        start_row = KS - 1 - offset
        filtered = (
            filtered
            + conv_weight[:, offset, None, :] * extended[:, start_row : start_row + tokens_here, :]
        )
    product = filtered[1] * filtered[2]

    return finish(filtered, product, decay_rate, residue, skip_gain, out_weight)


def finish(filtered, product, decay_rate, residue, skip_gain, out_weight):
    tokens_here, channels = product.shape
    modes = decay_rate.shape[0]
    rate = decay_rate
    mode_weight = residue * jnp.sqrt(-jnp.expm1(-2.0 * rate))
    lags = jnp.arange(tokens_here, dtype=jnp.float32)[:, None, None]
    growth = jnp.exp(rate[None] * lags)
    scaled = (growth * product[:, None, :]).reshape(tokens_here, modes * channels)
    lower = (jnp.arange(tokens_here)[:, None] >= jnp.arange(tokens_here)[None, :]).astype(jnp.float32)
    running = jnp.dot(lower, scaled, precision=PRECISE).reshape(tokens_here, modes, channels)
    local_state = jnp.exp(-rate * (tokens_here - 1)) * running[tokens_here - 1]
    section_entering = entering_state(local_state, rate, tokens_here, "seq")
    shrink = jnp.exp(-rate[None] * lags)
    total = running + jnp.exp(-rate) * section_entering
    long_part = jnp.sum(mode_weight[None] * shrink * total, axis=1)
    long_part = long_part + skip_gain[None, :] * product
    mixed_local = (filtered[0] * long_part).astype(jnp.bfloat16)
    groups = lax.axis_size("tensor")
    spread = jnp.broadcast_to(mixed_local[None], (groups,) + mixed_local.shape)
    features = lax.all_to_all(spread, "tensor", 0, 0)
    weight_all = lax.all_gather(out_weight, "seq", axis=0, tiled=True)
    weight_all = weight_all.reshape(groups, channels, weight_all.shape[1])
    projected = lax.dot_general(
        features,
        weight_all,
        (((0, 2), (0, 1)), ((), ())),
        preferred_element_type=jnp.float32,
    )
    return projected.astype(jnp.bfloat16)


def solution(mesh):
    return jax.shard_map(
        body,
        mesh=mesh,
        in_specs=(
            P(None, "seq", "tensor"),
            P(None, None, "tensor"),
            P(None, "tensor"),
            P(None, "tensor"),
            P("tensor"),
            P("seq", "tensor"),
        ),
        out_specs=P("seq", "tensor"),
        check_vma=False,
    )
```

```python
import jax
import jax.numpy as jnp
from jax import lax
from jax.sharding import PartitionSpec as P


KS = 3


PRECISE = lax.Precision.HIGHEST


def passed_along(block, axis, distance):
    devices = range(lax.axis_size(axis))
    route = [(i - distance, i) for i in devices if i - distance in devices]
    return lax.ppermute(block, axis, route)


def shifted(block, axis, route):
    return lax.ppermute(block, axis, route)


def ring_gather(block, axis, ring):
    size = lax.axis_size(axis)
    ring = min(ring, size)
    halves = size // ring
    place = lax.axis_index(axis)
    if halves == 2:
        partner = shifted(block, axis, [(i, i ^ ring) for i in range(size)])
        first = place // ring == 0
        chunk = jnp.where(first, jnp.stack([block, partner]), jnp.stack([partner, block]))
    else:
        chunk = block[None]
    forward = [(i, (i // ring) * ring + (i % ring + 1) % ring) for i in range(size)]
    backward = [(i, (i // ring) * ring + (i % ring - 1) % ring) for i in range(size)]
    ahead, behind = [], []
    up, down = chunk, chunk
    for step in range(ring // 2):
        up = shifted(up, axis, forward)
        behind.append(up)
        if step < (ring - 1) // 2:
            down = shifted(down, axis, backward)
            ahead.append(down)
    return jnp.stack([chunk] + ahead + behind[::-1])


def entering_state(local_state, rate, tokens_here, axis):
    sections = lax.axis_size(axis)
    decay = jnp.exp(-rate * tokens_here)
    state = passed_along(local_state, axis, 1)
    if sections > 2:
        state = state + decay * passed_along(local_state, axis, 2)
    distance = 2
    while distance < sections:
        state = state + jnp.exp(-rate * (tokens_here * distance)) * passed_along(state, axis, distance)
        distance *= 2
    return state


def body(qkv, conv_weight, decay_rate, residue, skip_gain, out_weight):
    tokens_here = qkv.shape[1]
    channels = qkv.shape[2]
    tail_rows = qkv[:, tokens_here - (KS - 1) :, :]
    previous = passed_along(tail_rows, "seq", 1)
    extended = jnp.concatenate([previous, qkv], axis=1).astype(jnp.float32)
    filtered = jnp.zeros((3, tokens_here, channels), jnp.float32)
    for offset in range(KS):
        start_row = KS - 1 - offset
        filtered = (
            filtered
            + conv_weight[:, offset, None, :] * extended[:, start_row : start_row + tokens_here, :]
        )
    product = filtered[1] * filtered[2]

    return finish(filtered, product, decay_rate, residue, skip_gain, out_weight)


def finish(filtered, product, decay_rate, residue, skip_gain, out_weight):
    tokens_here, channels = product.shape
    modes = decay_rate.shape[0]
    rate = decay_rate
    mode_weight = residue * jnp.sqrt(-jnp.expm1(-2.0 * rate))
    lags = jnp.arange(tokens_here, dtype=jnp.float32)[:, None, None]
    growth = jnp.exp(rate[None] * lags)
    scaled = (growth * product[:, None, :]).reshape(tokens_here, modes * channels)
    lower = (jnp.arange(tokens_here)[:, None] >= jnp.arange(tokens_here)[None, :]).astype(jnp.float32)
    running = jnp.dot(lower, scaled, precision=PRECISE).reshape(tokens_here, modes, channels)
    local_state = jnp.exp(-rate * (tokens_here - 1)) * running[tokens_here - 1]
    section_entering = entering_state(local_state, rate, tokens_here, "seq")
    shrink = jnp.exp(-rate[None] * lags)
    total = running + jnp.exp(-rate) * section_entering
    long_part = jnp.sum(mode_weight[None] * shrink * total, axis=1)
    long_part = long_part + skip_gain[None, :] * product
    mixed_local = (filtered[0] * long_part).astype(jnp.bfloat16)
    features = ring_gather(mixed_local, "tensor", 8)
    weight_all = lax.all_gather(out_weight, "seq", axis=0, tiled=True)
    ring = features.shape[0]
    halves = features.shape[1]
    weight_all = weight_all.reshape(halves, ring, channels, weight_all.shape[1])
    place = lax.axis_index("tensor") % ring
    weight_all = jnp.roll(weight_all, -place, axis=1)
    projected = jnp.einsum(
        "rhtc,hrco->to", features, weight_all, preferred_element_type=jnp.float32
    )
    return projected.astype(jnp.bfloat16)


def solution(mesh):
    return jax.shard_map(
        body,
        mesh=mesh,
        in_specs=(
            P(None, "seq", "tensor"),
            P(None, None, "tensor"),
            P(None, "tensor"),
            P(None, "tensor"),
            P("tensor"),
            P("seq", "tensor"),
        ),
        out_specs=P("seq", "tensor"),
        check_vma=False,
    )
```

```python
import jax
import jax.numpy as jnp
from jax import lax
from jax.sharding import PartitionSpec as P


KS = 3


PRECISE = lax.Precision.HIGHEST


def passed_along(block, axis, distance):
    devices = range(lax.axis_size(axis))
    route = [(i - distance, i) for i in devices if i - distance in devices]
    return lax.ppermute(block, axis, route)


def shifted(block, axis, route):
    return lax.ppermute(block, axis, route)


def ring_gather(block, axis, ring):
    size = lax.axis_size(axis)
    ring = min(ring, size)
    halves = size // ring
    place = lax.axis_index(axis)
    if halves == 2:
        partner = shifted(block, axis, [(i, i ^ ring) for i in range(size)])
        first = place // ring == 0
        chunk = jnp.where(first, jnp.stack([block, partner]), jnp.stack([partner, block]))
    else:
        chunk = block[None]
    forward = [(i, (i // ring) * ring + (i % ring + 1) % ring) for i in range(size)]
    backward = [(i, (i // ring) * ring + (i % ring - 1) % ring) for i in range(size)]
    ahead, behind = [], []
    up, down = chunk, chunk
    for step in range(ring // 2):
        up = shifted(up, axis, forward)
        behind.append(up)
        if step < (ring - 1) // 2:
            down = shifted(down, axis, backward)
            ahead.append(down)
    return [chunk] + ahead + behind[::-1]


def entering_state(local_state, rate, tokens_here, axis):
    sections = lax.axis_size(axis)
    state = jnp.zeros_like(local_state)
    for distance in range(1, min(4, sections - 1) + 1):
        lag = distance - 1
        state = state + jnp.exp(-rate * (tokens_here * lag)) * passed_along(local_state, axis, distance)
    width = 4
    while width < sections:
        grown = state
        for step in range(1, 4):
            distance = width * step
            if distance >= sections:
                break
            grown = grown + jnp.exp(-rate * (tokens_here * distance)) * passed_along(state, axis, distance)
        state = grown
        width *= 4
    return state


def body(qkv, conv_weight, decay_rate, residue, skip_gain, out_weight):
    tokens_here = qkv.shape[1]
    channels = qkv.shape[2]
    tail_rows = qkv[:, tokens_here - (KS - 1) :, :]
    previous = passed_along(tail_rows, "seq", 1)
    extended = jnp.concatenate([previous, qkv], axis=1).astype(jnp.float32)
    filtered = jnp.zeros((3, tokens_here, channels), jnp.float32)
    for offset in range(KS):
        start_row = KS - 1 - offset
        filtered = (
            filtered
            + conv_weight[:, offset, None, :] * extended[:, start_row : start_row + tokens_here, :]
        )
    product = filtered[1] * filtered[2]

    mixed_local = finish(filtered, product, decay_rate, residue, skip_gain)
    weight_parts, mixed_local = gather_weight(out_weight, channels, mixed_local)
    features = ring_gather(mixed_local, "tensor", 8)
    return project(features, weight_parts, out_weight.shape[-1])


def finish(filtered, product, decay_rate, residue, skip_gain):
    tokens_here, channels = product.shape
    modes = decay_rate.shape[0]
    rate = decay_rate
    mode_weight = residue * jnp.sqrt(-jnp.expm1(-2.0 * rate))
    lags = jnp.arange(tokens_here, dtype=jnp.float32)[:, None, None]
    local_state = jnp.sum(
        jnp.exp(-rate[None] * (tokens_here - 1 - lags)) * product[:, None, :], axis=0
    )
    section_entering = entering_state(local_state, rate, tokens_here, "seq")
    growth = jnp.exp(rate[None] * lags)
    scaled = (growth * product[:, None, :]).reshape(tokens_here, modes * channels)
    lower = (jnp.arange(tokens_here)[:, None] >= jnp.arange(tokens_here)[None, :]).astype(jnp.float32)
    running = jnp.dot(lower, scaled, precision=PRECISE).reshape(tokens_here, modes, channels)
    shrink = jnp.exp(-rate[None] * lags)
    inner = jnp.sum(mode_weight[None] * shrink * running, axis=1)
    carried = jnp.sum(
        (mode_weight * section_entering)[None] * jnp.exp(-rate[None] * (lags + 1.0)), axis=1
    )
    long_part = inner + carried
    long_part = long_part + skip_gain[None, :] * product
    return (filtered[0] * long_part).astype(jnp.bfloat16)


def gather_weight(out_weight, channels, later):
    sections = lax.axis_size("seq")
    rows = out_weight.shape[0]
    if 2 * rows != channels or sections % 2:
        return (lax.all_gather(out_weight, "seq", axis=0, tiled=True),), later
    parity_groups = [list(range(p, sections, 2)) for p in range(2)]
    mine = lax.all_gather(out_weight, "seq", axis=0, axis_index_groups=parity_groups)
    mine, later = lax.optimization_barrier((mine, later))
    other = shifted(mine, "seq", [(i, i ^ 1) for i in range(sections)])
    first = lax.axis_index("seq") % 2 == 0
    return (jnp.where(first, mine, other), jnp.where(first, other, mine)), later


def project(features, weight_parts, width):
    ring = len(features)
    halves = features[0].shape[0]
    tokens_here, channels = features[0].shape[1:]
    parts = len(weight_parts)
    piece = channels // parts
    blocks = [w.reshape(halves, ring, piece, width) for w in weight_parts]
    place = lax.axis_index("tensor") % ring
    projected = jnp.zeros((tokens_here, width), jnp.float32)
    for r in range(ring):
        index = (place + r) % ring
        for p, block in enumerate(blocks):
            taken = lax.dynamic_index_in_dim(block, index, 1, False)
            projected = projected + jnp.einsum(
                "htc,hco->to",
                features[r][..., p * piece : (p + 1) * piece],
                taken,
                preferred_element_type=jnp.float32,
            )
    return projected.astype(jnp.bfloat16)


def solution(mesh):
    return jax.shard_map(
        body,
        mesh=mesh,
        in_specs=(
            P(None, "seq", "tensor"),
            P(None, None, "tensor"),
            P(None, "tensor"),
            P(None, "tensor"),
            P("tensor"),
            P("seq", "tensor"),
        ),
        out_specs=P("seq", "tensor"),
        check_vma=False,
    )
```

```python
import jax
import jax.numpy as jnp
from jax import lax
from jax.sharding import PartitionSpec as P


KS = 3


PRECISE = lax.Precision.HIGHEST


def passed_along(block, axis, distance):
    devices = range(lax.axis_size(axis))
    route = [(i - distance, i) for i in devices if i - distance in devices]
    return lax.ppermute(block, axis, route)


def shifted(block, axis, route):
    return lax.ppermute(block, axis, route)


def ring_gather(block, axis, ring):
    size = lax.axis_size(axis)
    ring = min(ring, size)
    halves = size // ring
    place = lax.axis_index(axis)
    if halves == 2:
        partner = shifted(block, axis, [(i, i ^ ring) for i in range(size)])
        first = place // ring == 0
        chunk = jnp.where(first, jnp.stack([block, partner]), jnp.stack([partner, block]))
    else:
        chunk = block[None]
    forward = [(i, (i // ring) * ring + (i % ring + 1) % ring) for i in range(size)]
    backward = [(i, (i // ring) * ring + (i % ring - 1) % ring) for i in range(size)]
    ahead, behind = [], []
    up, down = chunk, chunk
    for step in range(ring // 2):
        up = shifted(up, axis, forward)
        behind.append(up)
        if step < (ring - 1) // 2:
            down = shifted(down, axis, backward)
            ahead.append(down)
    return [chunk] + ahead + behind[::-1]


def entering_state(local_state, rate, tokens_here, axis):
    sections = lax.axis_size(axis)
    state = jnp.zeros_like(local_state)
    for distance in range(1, min(4, sections - 1) + 1):
        lag = distance - 1
        state = state + jnp.exp(-rate * (tokens_here * lag)) * passed_along(local_state, axis, distance)
    width = 4
    while width < sections:
        grown = state
        for step in range(1, 4):
            distance = width * step
            if distance >= sections:
                break
            grown = grown + jnp.exp(-rate * (tokens_here * distance)) * passed_along(state, axis, distance)
        state = grown
        width *= 4
    return state


def body(qkv, conv_weight, decay_rate, residue, skip_gain, out_weight):
    tokens_here = qkv.shape[1]
    channels = qkv.shape[2]
    tail_rows = qkv[:, tokens_here - (KS - 1) :, :]
    previous = passed_along(tail_rows, "seq", 1)
    extended = jnp.concatenate([previous, qkv], axis=1).astype(jnp.float32)
    filtered = jnp.zeros((3, tokens_here, channels), jnp.float32)
    for offset in range(KS):
        start_row = KS - 1 - offset
        filtered = (
            filtered
            + conv_weight[:, offset, None, :] * extended[:, start_row : start_row + tokens_here, :]
        )
    product = filtered[1] * filtered[2]

    return finish(filtered, product, decay_rate, residue, skip_gain, out_weight)


def finish(filtered, product, decay_rate, residue, skip_gain, out_weight):
    tokens_here, channels = product.shape
    modes = decay_rate.shape[0]
    rate = decay_rate
    mode_weight = residue * jnp.sqrt(-jnp.expm1(-2.0 * rate))
    lags = jnp.arange(tokens_here, dtype=jnp.float32)[:, None, None]
    local_state = jnp.sum(
        jnp.exp(-rate[None] * (tokens_here - 1 - lags)) * product[:, None, :], axis=0
    )
    section_entering = entering_state(local_state, rate, tokens_here, "seq")
    growth = jnp.exp(rate[None] * lags)
    scaled = (growth * product[:, None, :]).reshape(tokens_here, modes * channels)
    lower = (jnp.arange(tokens_here)[:, None] >= jnp.arange(tokens_here)[None, :]).astype(jnp.float32)
    running = jnp.dot(lower, scaled, precision=PRECISE).reshape(tokens_here, modes, channels)
    shrink = jnp.exp(-rate[None] * lags)
    inner = jnp.sum(mode_weight[None] * shrink * running, axis=1)
    carried = jnp.sum(
        (mode_weight * section_entering)[None] * jnp.exp(-rate[None] * (lags + 1.0)), axis=1
    )
    long_part = inner + carried
    long_part = long_part + skip_gain[None, :] * product
    mixed_local = (filtered[0] * long_part).astype(jnp.bfloat16)
    features = ring_gather(mixed_local, "tensor", 8)
    weight_all = lax.all_gather(out_weight, "seq", axis=0, tiled=True)
    ring = len(features)
    halves = features[0].shape[0]
    weight_all = weight_all.reshape(halves, ring, channels, weight_all.shape[1])
    place = lax.axis_index("tensor") % ring
    projected = jnp.zeros((features[0].shape[1], weight_all.shape[-1]), jnp.float32)
    for r in range(ring):
        taken = lax.dynamic_index_in_dim(weight_all, (place + r) % ring, 1, False)
        projected = projected + jnp.einsum(
            "htc,hco->to", features[r], taken, preferred_element_type=jnp.float32
        )
    return projected.astype(jnp.bfloat16)


def solution(mesh):
    return jax.shard_map(
        body,
        mesh=mesh,
        in_specs=(
            P(None, "seq", "tensor"),
            P(None, None, "tensor"),
            P(None, "tensor"),
            P(None, "tensor"),
            P("tensor"),
            P("seq", "tensor"),
        ),
        out_specs=P("seq", "tensor"),
        check_vma=False,
    )
```

```python
import jax
import jax.numpy as jnp
from jax import lax
from jax.sharding import PartitionSpec as P


KS = 3


PRECISE = lax.Precision.HIGHEST


def passed_along(block, axis, distance):
    devices = range(lax.axis_size(axis))
    route = [(i - distance, i) for i in devices if i - distance in devices]
    return lax.ppermute(block, axis, route)


def shifted(block, axis, route):
    return lax.ppermute(block, axis, route)


def ring_gather(block, axis, ring):
    size = lax.axis_size(axis)
    ring = min(ring, size)
    halves = size // ring
    place = lax.axis_index(axis)
    if halves == 2:
        partner = shifted(block, axis, [(i, i ^ ring) for i in range(size)])
        first = place // ring == 0
        chunk = jnp.where(first, jnp.stack([block, partner]), jnp.stack([partner, block]))
    else:
        chunk = block[None]
    forward = [(i, (i // ring) * ring + (i % ring + 1) % ring) for i in range(size)]
    backward = [(i, (i // ring) * ring + (i % ring - 1) % ring) for i in range(size)]
    ahead, behind = [], []
    up, down = chunk, chunk
    for step in range(ring // 2):
        up = shifted(up, axis, forward)
        behind.append(up)
        if step < (ring - 1) // 2:
            down = shifted(down, axis, backward)
            ahead.append(down)
    return [chunk] + ahead + behind[::-1]


def entering_state(local_state, rate, tokens_here, axis):
    sections = lax.axis_size(axis)
    state = jnp.zeros_like(local_state)
    for distance in range(1, min(4, sections - 1) + 1):
        lag = distance - 1
        state = state + jnp.exp(-rate * (tokens_here * lag)) * passed_along(local_state, axis, distance)
    width = 4
    while width < sections:
        grown = state
        for step in range(1, 4):
            distance = width * step
            if distance >= sections:
                break
            grown = grown + jnp.exp(-rate * (tokens_here * distance)) * passed_along(state, axis, distance)
        state = grown
        width *= 4
    return state


def body(qkv, conv_weight, decay_rate, residue, skip_gain, out_weight):
    tokens_here = qkv.shape[1]
    channels = qkv.shape[2]
    tail_rows = qkv[:, tokens_here - (KS - 1) :, :]
    previous = passed_along(tail_rows, "seq", 1)
    extended = jnp.concatenate([previous, qkv], axis=1).astype(jnp.float32)
    filtered = jnp.zeros((3, tokens_here, channels), jnp.float32)
    for offset in range(KS):
        start_row = KS - 1 - offset
        filtered = (
            filtered
            + conv_weight[:, offset, None, :] * extended[:, start_row : start_row + tokens_here, :]
        )
    product = filtered[1] * filtered[2]

    mixed_local = finish(filtered, product, decay_rate, residue, skip_gain)
    return tail(mixed_local, out_weight)


def finish(filtered, product, decay_rate, residue, skip_gain):
    tokens_here, channels = product.shape
    modes = decay_rate.shape[0]
    rate = decay_rate
    mode_weight = residue * jnp.sqrt(-jnp.expm1(-2.0 * rate))
    lags = jnp.arange(tokens_here, dtype=jnp.float32)[:, None, None]
    local_state = jnp.sum(
        jnp.exp(-rate[None] * (tokens_here - 1 - lags)) * product[:, None, :], axis=0
    )
    section_entering = entering_state(local_state, rate, tokens_here, "seq")
    growth = jnp.exp(rate[None] * lags)
    scaled = (growth * product[:, None, :]).reshape(tokens_here, modes * channels)
    lower = (jnp.arange(tokens_here)[:, None] >= jnp.arange(tokens_here)[None, :]).astype(jnp.float32)
    running = jnp.dot(lower, scaled, precision=PRECISE).reshape(tokens_here, modes, channels)
    shrink = jnp.exp(-rate[None] * lags)
    inner = jnp.sum(mode_weight[None] * shrink * running, axis=1)
    carried = jnp.sum(
        (mode_weight * section_entering)[None] * jnp.exp(-rate[None] * (lags + 1.0)), axis=1
    )
    long_part = inner + carried
    long_part = long_part + skip_gain[None, :] * product
    return (filtered[0] * long_part).astype(jnp.bfloat16)


def tail(mixed_local, out_weight):
    channels = mixed_local.shape[1]
    features = ring_gather(mixed_local, "tensor", 8)
    weight_all = lax.all_gather(out_weight, "seq", axis=0, tiled=True)
    ring = len(features)
    halves = features[0].shape[0]
    weight_all = weight_all.reshape(halves, ring, channels, weight_all.shape[1])
    place = lax.axis_index("tensor") % ring
    projected = jnp.zeros((features[0].shape[1], weight_all.shape[-1]), jnp.float32)
    for r in range(ring):
        taken = lax.dynamic_index_in_dim(weight_all, (place + r) % ring, 1, False)
        projected = projected + jnp.einsum(
            "htc,hco->to", features[r], taken, preferred_element_type=jnp.float32
        )
    return projected.astype(jnp.bfloat16)


def solution(mesh):
    return jax.shard_map(
        body,
        mesh=mesh,
        in_specs=(
            P(None, "seq", "tensor"),
            P(None, None, "tensor"),
            P(None, "tensor"),
            P(None, "tensor"),
            P("tensor"),
            P("seq", "tensor"),
        ),
        out_specs=P("seq", "tensor"),
        check_vma=False,
    )
```

```python
import jax
import jax.numpy as jnp
from jax import lax
from jax.sharding import PartitionSpec as P


KS = 3


PRECISE = lax.Precision.HIGHEST


def passed_along(block, axis, distance):
    devices = range(lax.axis_size(axis))
    route = [(i - distance, i) for i in devices if i - distance in devices]
    return lax.ppermute(block, axis, route)


def shifted(block, axis, route):
    return lax.ppermute(block, axis, route)


def ring_gather(block, axis, ring):
    size = lax.axis_size(axis)
    ring = min(ring, size)
    halves = size // ring
    place = lax.axis_index(axis)
    if halves == 2:
        partner = shifted(block, axis, [(i, i ^ ring) for i in range(size)])
        first = place // ring == 0
        chunk = jnp.where(first, jnp.stack([block, partner]), jnp.stack([partner, block]))
    else:
        chunk = block[None]
    forward = [(i, (i // ring) * ring + (i % ring + 1) % ring) for i in range(size)]
    backward = [(i, (i // ring) * ring + (i % ring - 1) % ring) for i in range(size)]
    ahead, behind = [], []
    up, down = chunk, chunk
    for step in range(ring // 2):
        up = shifted(up, axis, forward)
        behind.append(up)
        if step < (ring - 1) // 2:
            down = shifted(down, axis, backward)
            ahead.append(down)
    return [chunk] + ahead + behind[::-1]


def entering_state(local_state, rate, tokens_here, axis):
    sections = lax.axis_size(axis)
    spread = jnp.broadcast_to(local_state[None], (sections,) + local_state.shape)
    states = lax.all_to_all(spread, axis, 0, 0)
    here = lax.axis_index(axis)
    earlier = jnp.arange(sections)
    lag = jnp.maximum(here - 1 - earlier, 0).astype(jnp.float32)[:, None, None]
    weight = jnp.exp(-rate[None] * (tokens_here * lag))
    taken = (earlier < here)[:, None, None]
    return jnp.sum(jnp.where(taken, weight * states, 0.0), axis=0)


def body(qkv, conv_weight, decay_rate, residue, skip_gain, out_weight):
    tokens_here = qkv.shape[1]
    channels = qkv.shape[2]
    tail_rows = qkv[:, tokens_here - (KS - 1) :, :]
    previous = passed_along(tail_rows, "seq", 1)
    extended = jnp.concatenate([previous, qkv], axis=1).astype(jnp.float32)
    filtered = jnp.zeros((3, tokens_here, channels), jnp.float32)
    for offset in range(KS):
        start_row = KS - 1 - offset
        filtered = (
            filtered
            + conv_weight[:, offset, None, :] * extended[:, start_row : start_row + tokens_here, :]
        )
    product = filtered[1] * filtered[2]

    mixed_local = finish(filtered, product, decay_rate, residue, skip_gain)
    return tail(mixed_local, out_weight)


def finish(filtered, product, decay_rate, residue, skip_gain):
    tokens_here, channels = product.shape
    modes = decay_rate.shape[0]
    rate = decay_rate
    mode_weight = residue * jnp.sqrt(-jnp.expm1(-2.0 * rate))
    lags = jnp.arange(tokens_here, dtype=jnp.float32)[:, None, None]
    local_state = jnp.sum(
        jnp.exp(-rate[None] * (tokens_here - 1 - lags)) * product[:, None, :], axis=0
    )
    section_entering = entering_state(local_state, rate, tokens_here, "seq")
    growth = jnp.exp(rate[None] * lags)
    scaled = (growth * product[:, None, :]).reshape(tokens_here, modes * channels)
    lower = (jnp.arange(tokens_here)[:, None] >= jnp.arange(tokens_here)[None, :]).astype(jnp.float32)
    running = jnp.dot(lower, scaled, precision=PRECISE).reshape(tokens_here, modes, channels)
    shrink = jnp.exp(-rate[None] * lags)
    inner = jnp.sum(mode_weight[None] * shrink * running, axis=1)
    carried = jnp.sum(
        (mode_weight * section_entering)[None] * jnp.exp(-rate[None] * (lags + 1.0)), axis=1
    )
    long_part = inner + carried
    long_part = long_part + skip_gain[None, :] * product
    return (filtered[0] * long_part).astype(jnp.bfloat16)


def tail(mixed_local, out_weight):
    channels = mixed_local.shape[1]
    features = ring_gather(mixed_local, "tensor", 8)
    weight_all = lax.all_gather(out_weight, "seq", axis=0, tiled=True)
    ring = len(features)
    halves = features[0].shape[0]
    weight_all = weight_all.reshape(halves, ring, channels, weight_all.shape[1])
    place = lax.axis_index("tensor") % ring
    projected = jnp.zeros((features[0].shape[1], weight_all.shape[-1]), jnp.float32)
    for r in range(ring):
        taken = lax.dynamic_index_in_dim(weight_all, (place + r) % ring, 1, False)
        projected = projected + jnp.einsum(
            "htc,hco->to", features[r], taken, preferred_element_type=jnp.float32
        )
    return projected.astype(jnp.bfloat16)


def solution(mesh):
    return jax.shard_map(
        body,
        mesh=mesh,
        in_specs=(
            P(None, "seq", "tensor"),
            P(None, None, "tensor"),
            P(None, "tensor"),
            P(None, "tensor"),
            P("tensor"),
            P("seq", "tensor"),
        ),
        out_specs=P("seq", "tensor"),
        check_vma=False,
    )
```

```python
import jax
import jax.numpy as jnp
from jax import lax
from jax.sharding import PartitionSpec as P


KS = 3


PRECISE = lax.Precision.HIGHEST


def passed_along(block, axis, distance):
    devices = range(lax.axis_size(axis))
    route = [(i - distance, i) for i in devices if i - distance in devices]
    return lax.ppermute(block, axis, route)


def shifted(block, axis, route):
    return lax.ppermute(block, axis, route)


def ring_gather(block, axis, ring):
    size = lax.axis_size(axis)
    ring = min(ring, size)
    halves = size // ring
    place = lax.axis_index(axis)
    if halves == 2:
        partner = shifted(block, axis, [(i, i ^ ring) for i in range(size)])
        first = place // ring == 0
        chunk = jnp.where(first, jnp.stack([block, partner]), jnp.stack([partner, block]))
    else:
        chunk = block[None]
    forward = [(i, (i // ring) * ring + (i % ring + 1) % ring) for i in range(size)]
    backward = [(i, (i // ring) * ring + (i % ring - 1) % ring) for i in range(size)]
    ahead, behind = [], []
    up, down = chunk, chunk
    for step in range(ring // 2):
        if step < (ring - 1) // 2:
            up = shifted(up, axis, forward)
            behind.append(up)
            down = shifted(down, axis, backward)
            ahead.append(down)
        elif halves == 2:
            up = shifted(up[:1], axis, forward)
            down = shifted(down[1:], axis, backward)
            behind.append(jnp.concatenate([up, down]))
        else:
            up = shifted(up, axis, forward)
            behind.append(up)
    return [chunk] + ahead + behind[::-1]


def entering_state(local_state, rate, tokens_here, axis):
    sections = lax.axis_size(axis)
    state = jnp.zeros_like(local_state)
    for distance in range(1, min(4, sections - 1) + 1):
        lag = distance - 1
        state = state + jnp.exp(-rate * (tokens_here * lag)) * passed_along(local_state, axis, distance)
    width = 4
    while width < sections:
        grown = state
        for step in range(1, 4):
            distance = width * step
            if distance >= sections:
                break
            grown = grown + jnp.exp(-rate * (tokens_here * distance)) * passed_along(state, axis, distance)
        state = grown
        width *= 4
    return state


def body(qkv, conv_weight, decay_rate, residue, skip_gain, out_weight):
    tokens_here = qkv.shape[1]
    channels = qkv.shape[2]
    tail_rows = qkv[:, tokens_here - (KS - 1) :, :]
    previous = passed_along(tail_rows, "seq", 1)
    extended = jnp.concatenate([previous, qkv], axis=1).astype(jnp.float32)
    filtered = jnp.zeros((3, tokens_here, channels), jnp.float32)
    for offset in range(KS):
        start_row = KS - 1 - offset
        filtered = (
            filtered
            + conv_weight[:, offset, None, :] * extended[:, start_row : start_row + tokens_here, :]
        )
    product = filtered[1] * filtered[2]

    mixed_local = finish(filtered, product, decay_rate, residue, skip_gain)
    return tail(mixed_local, out_weight)


def finish(filtered, product, decay_rate, residue, skip_gain):
    tokens_here, channels = product.shape
    modes = decay_rate.shape[0]
    rate = decay_rate
    mode_weight = residue * jnp.sqrt(-jnp.expm1(-2.0 * rate))
    lags = jnp.arange(tokens_here, dtype=jnp.float32)[:, None, None]
    local_state = jnp.sum(
        jnp.exp(-rate[None] * (tokens_here - 1 - lags)) * product[:, None, :], axis=0
    )
    section_entering = entering_state(local_state, rate, tokens_here, "seq")
    growth = jnp.exp(rate[None] * lags)
    scaled = (growth * product[:, None, :]).reshape(tokens_here, modes * channels)
    lower = (jnp.arange(tokens_here)[:, None] >= jnp.arange(tokens_here)[None, :]).astype(jnp.float32)
    running = jnp.dot(lower, scaled, precision=PRECISE).reshape(tokens_here, modes, channels)
    shrink = jnp.exp(-rate[None] * lags)
    inner = jnp.sum(mode_weight[None] * shrink * running, axis=1)
    carried = jnp.sum(
        (mode_weight * section_entering)[None] * jnp.exp(-rate[None] * (lags + 1.0)), axis=1
    )
    long_part = inner + carried
    long_part = long_part + skip_gain[None, :] * product
    return (filtered[0] * long_part).astype(jnp.bfloat16)


def tail(mixed_local, out_weight):
    channels = mixed_local.shape[1]
    features = ring_gather(mixed_local, "tensor", 8)
    weight_all = lax.all_gather(out_weight, "seq", axis=0, tiled=True)
    ring = len(features)
    halves = features[0].shape[0]
    weight_all = weight_all.reshape(halves, ring, channels, weight_all.shape[1])
    place = lax.axis_index("tensor") % ring
    projected = jnp.zeros((features[0].shape[1], weight_all.shape[-1]), jnp.float32)
    for r in range(ring):
        taken = lax.dynamic_index_in_dim(weight_all, (place + r) % ring, 1, False)
        projected = projected + jnp.einsum(
            "htc,hco->to", features[r], taken, preferred_element_type=jnp.float32
        )
    return projected.astype(jnp.bfloat16)


def solution(mesh):
    return jax.shard_map(
        body,
        mesh=mesh,
        in_specs=(
            P(None, "seq", "tensor"),
            P(None, None, "tensor"),
            P(None, "tensor"),
            P(None, "tensor"),
            P("tensor"),
            P("seq", "tensor"),
        ),
        out_specs=P("seq", "tensor"),
        check_vma=False,
    )
```

```python
import jax
import jax.numpy as jnp
from jax import lax
from jax.sharding import PartitionSpec as P


KS = 3


PRECISE = lax.Precision.HIGHEST


def passed_along(block, axis, distance):
    devices = range(lax.axis_size(axis))
    route = [(i - distance, i) for i in devices if i - distance in devices]
    return lax.ppermute(block, axis, route)


def shifted(block, axis, route):
    return lax.ppermute(block, axis, route)


def ring_gather(block, axis, ring):
    size = lax.axis_size(axis)
    ring = min(ring, size)
    halves = size // ring
    place = lax.axis_index(axis)
    if halves == 2:
        partner = shifted(block, axis, [(i, i ^ ring) for i in range(size)])
        first = place // ring == 0
        chunk = jnp.where(first, jnp.stack([block, partner]), jnp.stack([partner, block]))
    else:
        chunk = block[None]
    forward = [(i, (i // ring) * ring + (i % ring + 1) % ring) for i in range(size)]
    backward = [(i, (i // ring) * ring + (i % ring - 1) % ring) for i in range(size)]
    ahead, behind = [], []
    up, down = chunk, chunk
    for step in range(ring // 2):
        up = shifted(up, axis, forward)
        behind.append(up)
        if step < (ring - 1) // 2:
            down = shifted(down, axis, backward)
            ahead.append(down)
    return [chunk] + ahead + behind[::-1]


def entering_state(local_state, rate, tokens_here, axis):
    sections = lax.axis_size(axis)
    state = jnp.zeros_like(local_state)
    for distance in range(1, min(4, sections - 1) + 1):
        lag = distance - 1
        state = state + jnp.exp(-rate * (tokens_here * lag)) * passed_along(local_state, axis, distance)
    width = 4
    while width < sections:
        grown = state
        for step in range(1, 4):
            distance = width * step
            if distance >= sections:
                break
            grown = grown + jnp.exp(-rate * (tokens_here * distance)) * passed_along(state, axis, distance)
        state = grown
        width *= 4
    return state


def body(qkv, conv_weight, decay_rate, residue, skip_gain, out_weight):
    tokens_here = qkv.shape[1]
    channels = qkv.shape[2]
    tail_rows = qkv[:, tokens_here - (KS - 1) :, :]
    previous = passed_along(tail_rows, "seq", 1)
    extended = jnp.concatenate([previous, qkv], axis=1).astype(jnp.float32)
    filtered = jnp.zeros((3, tokens_here, channels), jnp.float32)
    for offset in range(KS):
        start_row = KS - 1 - offset
        filtered = (
            filtered
            + conv_weight[:, offset, None, :] * extended[:, start_row : start_row + tokens_here, :]
        )
    product = filtered[1] * filtered[2]

    mixed_local = finish(filtered, product, decay_rate, residue, skip_gain)
    return tail(mixed_local, out_weight)


def finish(filtered, product, decay_rate, residue, skip_gain):
    tokens_here, channels = product.shape
    modes = decay_rate.shape[0]
    rate = decay_rate
    mode_weight = residue * jnp.sqrt(-jnp.expm1(-2.0 * rate))
    lags = jnp.arange(tokens_here, dtype=jnp.float32)[:, None, None]
    local_state = jnp.sum(
        jnp.exp(-rate[None] * (tokens_here - 1 - lags)) * product[:, None, :], axis=0
    )
    section_entering = entering_state(local_state, rate, tokens_here, "seq")
    growth = jnp.exp(rate[None] * lags)
    scaled = (growth * product[:, None, :]).reshape(tokens_here, modes * channels)
    lower = (jnp.arange(tokens_here)[:, None] >= jnp.arange(tokens_here)[None, :]).astype(jnp.float32)
    running = jnp.dot(lower, scaled, precision=PRECISE).reshape(tokens_here, modes, channels)
    shrink = jnp.exp(-rate[None] * lags)
    inner = jnp.sum(mode_weight[None] * shrink * running, axis=1)
    carried = jnp.sum(
        (mode_weight * section_entering)[None] * jnp.exp(-rate[None] * (lags + 1.0)), axis=1
    )
    long_part = inner + carried
    long_part = long_part + skip_gain[None, :] * product
    return (filtered[0] * long_part).astype(jnp.bfloat16)


def tail(mixed_local, out_weight):
    channels = mixed_local.shape[1]
    features = ring_gather(mixed_local, "tensor", 8)
    sections = lax.axis_size("seq")
    spread = jnp.broadcast_to(out_weight[None], (sections,) + out_weight.shape)
    weight_all = lax.all_to_all(spread, "seq", 0, 0)
    weight_all = weight_all.reshape(sections * out_weight.shape[0], out_weight.shape[1])
    ring = len(features)
    halves = features[0].shape[0]
    weight_all = weight_all.reshape(halves, ring, channels, weight_all.shape[1])
    place = lax.axis_index("tensor") % ring
    projected = jnp.zeros((features[0].shape[1], weight_all.shape[-1]), jnp.float32)
    for r in range(ring):
        taken = lax.dynamic_index_in_dim(weight_all, (place + r) % ring, 1, False)
        projected = projected + jnp.einsum(
            "htc,hco->to", features[r], taken, preferred_element_type=jnp.float32
        )
    return projected.astype(jnp.bfloat16)


def solution(mesh):
    return jax.shard_map(
        body,
        mesh=mesh,
        in_specs=(
            P(None, "seq", "tensor"),
            P(None, None, "tensor"),
            P(None, "tensor"),
            P(None, "tensor"),
            P("tensor"),
            P("seq", "tensor"),
        ),
        out_specs=P("seq", "tensor"),
        check_vma=False,
    )
```

```python
import jax
import jax.numpy as jnp
from jax import lax
from jax.sharding import PartitionSpec as P


KS = 3


PRECISE = lax.Precision.HIGHEST


def passed_along(block, axis, distance):
    devices = range(lax.axis_size(axis))
    route = [(i - distance, i) for i in devices if i - distance in devices]
    return lax.ppermute(block, axis, route)


def shifted(block, axis, route):
    return lax.ppermute(block, axis, route)


def ring_gather(block, axis, ring):
    size = lax.axis_size(axis)
    ring = min(ring, size)
    halves = size // ring
    place = lax.axis_index(axis)
    forward = [(i, (i // ring) * ring + (i % ring + 1) % ring) for i in range(size)]
    backward = [(i, (i // ring) * ring + (i % ring - 1) % ring) for i in range(size)]
    up_steps, down_steps = ring // 2, (ring - 1) // 2
    if halves != 2:
        ahead, behind = [], []
        up, down = block, block
        for step in range(up_steps):
            up = shifted(up, axis, forward)
            behind.append(up)
            if step < down_steps:
                down = shifted(down, axis, backward)
                ahead.append(down)
        return [c[None] for c in [block] + ahead + behind[::-1]]
    partner = shifted(block, axis, [(i, i ^ ring) for i in range(size)])
    own_up, own_down, far_up, far_down = [], [], [], []
    cur = {"ou": block, "od": block, "fu": partner, "fd": partner}
    for rnd in range(up_steps + 1):
        up_parts, down_parts = [], []
        if rnd < up_steps:
            up_parts.append("ou")
        if rnd < down_steps:
            down_parts.append("od")
        if 1 <= rnd <= up_steps:
            up_parts.append("fu")
        if 1 <= rnd <= down_steps:
            down_parts.append("fd")
        for parts, route in ((up_parts, forward), (down_parts, backward)):
            if not parts:
                continue
            moved = shifted(jnp.stack([cur[p] for p in parts]), axis, route)
            for n, p in enumerate(parts):
                cur[p] = moved[n]
                {"ou": own_up, "od": own_down, "fu": far_up, "fd": far_down}[p].append(moved[n])
    first = place // ring == 0

    def pair(own, far):
        return jnp.where(first, jnp.stack([own, far]), jnp.stack([far, own]))

    chunks = [pair(block, partner)]
    chunks += [pair(o, f) for o, f in zip(own_down, far_down)]
    chunks += [pair(o, f) for o, f in zip(own_up, far_up)][::-1]
    return chunks


def entering_state(local_state, rate, tokens_here, axis):
    sections = lax.axis_size(axis)
    state = jnp.zeros_like(local_state)
    for distance in range(1, min(4, sections - 1) + 1):
        lag = distance - 1
        state = state + jnp.exp(-rate * (tokens_here * lag)) * passed_along(local_state, axis, distance)
    width = 4
    while width < sections:
        grown = state
        for step in range(1, 4):
            distance = width * step
            if distance >= sections:
                break
            grown = grown + jnp.exp(-rate * (tokens_here * distance)) * passed_along(state, axis, distance)
        state = grown
        width *= 4
    return state


def body(qkv, conv_weight, decay_rate, residue, skip_gain, out_weight):
    tokens_here = qkv.shape[1]
    channels = qkv.shape[2]
    tail_rows = qkv[:, tokens_here - (KS - 1) :, :]
    previous = passed_along(tail_rows, "seq", 1)
    extended = jnp.concatenate([previous, qkv], axis=1).astype(jnp.float32)
    filtered = jnp.zeros((3, tokens_here, channels), jnp.float32)
    for offset in range(KS):
        start_row = KS - 1 - offset
        filtered = (
            filtered
            + conv_weight[:, offset, None, :] * extended[:, start_row : start_row + tokens_here, :]
        )
    product = filtered[1] * filtered[2]

    return finish(filtered, product, decay_rate, residue, skip_gain, out_weight)


def finish(filtered, product, decay_rate, residue, skip_gain, out_weight):
    tokens_here, channels = product.shape
    modes = decay_rate.shape[0]
    rate = decay_rate
    mode_weight = residue * jnp.sqrt(-jnp.expm1(-2.0 * rate))
    lags = jnp.arange(tokens_here, dtype=jnp.float32)[:, None, None]
    local_state = jnp.sum(
        jnp.exp(-rate[None] * (tokens_here - 1 - lags)) * product[:, None, :], axis=0
    )
    section_entering = entering_state(local_state, rate, tokens_here, "seq")
    growth = jnp.exp(rate[None] * lags)
    scaled = (growth * product[:, None, :]).reshape(tokens_here, modes * channels)
    lower = (jnp.arange(tokens_here)[:, None] >= jnp.arange(tokens_here)[None, :]).astype(jnp.float32)
    running = jnp.dot(lower, scaled, precision=PRECISE).reshape(tokens_here, modes, channels)
    shrink = jnp.exp(-rate[None] * lags)
    inner = jnp.sum(mode_weight[None] * shrink * running, axis=1)
    carried = jnp.sum(
        (mode_weight * section_entering)[None] * jnp.exp(-rate[None] * (lags + 1.0)), axis=1
    )
    long_part = inner + carried
    long_part = long_part + skip_gain[None, :] * product
    mixed_local = (filtered[0] * long_part).astype(jnp.bfloat16)
    features = ring_gather(mixed_local, "tensor", 8)
    weight_all = lax.all_gather(out_weight, "seq", axis=0, tiled=True)
    ring = len(features)
    halves = features[0].shape[0]
    weight_all = weight_all.reshape(halves, ring, channels, weight_all.shape[1])
    place = lax.axis_index("tensor") % ring
    weight_all = jnp.roll(weight_all, -place, axis=1)
    projected = jnp.zeros((features[0].shape[1], weight_all.shape[-1]), jnp.float32)
    for r in range(ring):
        projected = projected + jnp.einsum(
            "htc,hco->to", features[r], weight_all[:, r], preferred_element_type=jnp.float32
        )
    return projected.astype(jnp.bfloat16)


def solution(mesh):
    return jax.shard_map(
        body,
        mesh=mesh,
        in_specs=(
            P(None, "seq", "tensor"),
            P(None, None, "tensor"),
            P(None, "tensor"),
            P(None, "tensor"),
            P("tensor"),
            P("seq", "tensor"),
        ),
        out_specs=P("seq", "tensor"),
        check_vma=False,
    )
```

```python
import jax
import jax.numpy as jnp
from jax import lax
from jax.sharding import PartitionSpec as P


KS = 3


def passed_along(block, axis, distance):
    devices = range(lax.axis_size(axis))
    route = [(i - distance, i) for i in devices if i - distance in devices]
    return lax.ppermute(block, axis, route)


def shifted(block, axis, route):
    return lax.ppermute(block, axis, route)


def ring_gather(block, axis, ring):
    size = lax.axis_size(axis)
    ring = min(ring, size)
    halves = size // ring
    place = lax.axis_index(axis)
    if halves == 2:
        partner = shifted(block, axis, [(i, i ^ ring) for i in range(size)])
        first = place // ring == 0
        chunk = jnp.where(first, jnp.stack([block, partner]), jnp.stack([partner, block]))
    else:
        chunk = block[None]
    forward = [(i, (i // ring) * ring + (i % ring + 1) % ring) for i in range(size)]
    backward = [(i, (i // ring) * ring + (i % ring - 1) % ring) for i in range(size)]
    ahead, behind = [], []
    up, down = chunk, chunk
    for step in range(ring // 2):
        up = shifted(up, axis, forward)
        behind.append(up)
        if step < (ring - 1) // 2:
            down = shifted(down, axis, backward)
            ahead.append(down)
    return [chunk] + ahead + behind[::-1]


def entering_state(local_state, rate, tokens_here, axis):
    sections = lax.axis_size(axis)
    state = jnp.zeros_like(local_state)
    for distance in range(1, min(4, sections - 1) + 1):
        lag = distance - 1
        state = state + jnp.exp(-rate * (tokens_here * lag)) * passed_along(local_state, axis, distance)
    width = 4
    while width < sections:
        grown = state
        for step in range(1, 4):
            distance = width * step
            if distance >= sections:
                break
            grown = grown + jnp.exp(-rate * (tokens_here * distance)) * passed_along(state, axis, distance)
        state = grown
        width *= 4
    return state


def body(qkv, conv_weight, decay_rate, residue, skip_gain, out_weight):
    tokens_here = qkv.shape[1]
    channels = qkv.shape[2]
    tail_rows = qkv[:, tokens_here - (KS - 1) :, :]
    previous = passed_along(tail_rows, "seq", 1)
    extended = jnp.concatenate([previous, qkv], axis=1).astype(jnp.float32)
    filtered = jnp.zeros((3, tokens_here, channels), jnp.float32)
    for offset in range(KS):
        start_row = KS - 1 - offset
        filtered = (
            filtered
            + conv_weight[:, offset, None, :] * extended[:, start_row : start_row + tokens_here, :]
        )
    product = filtered[1] * filtered[2]

    return finish(filtered, product, decay_rate, residue, skip_gain, out_weight)


def finish(filtered, product, decay_rate, residue, skip_gain, out_weight):
    tokens_here, channels = product.shape
    modes = decay_rate.shape[0]
    rate = decay_rate
    mode_weight = residue * jnp.sqrt(-jnp.expm1(-2.0 * rate))
    lags = jnp.arange(tokens_here, dtype=jnp.float32)[:, None, None]
    local_state = jnp.sum(
        jnp.exp(-rate[None] * (tokens_here - 1 - lags)) * product[:, None, :], axis=0
    )
    section_entering = entering_state(local_state, rate, tokens_here, "seq")
    growth = jnp.exp(rate[None] * lags)
    scaled = (growth * product[:, None, :]).reshape(tokens_here, modes * channels)
    lower = (jnp.arange(tokens_here)[:, None] >= jnp.arange(tokens_here)[None, :]).astype(jnp.float32)
    running = jnp.dot(lower, scaled, precision=lax.Precision.HIGH).reshape(tokens_here, modes, channels)
    shrink = jnp.exp(-rate[None] * lags)
    inner = jnp.sum(mode_weight[None] * shrink * running, axis=1)
    carried = jnp.sum(
        (mode_weight * section_entering)[None] * jnp.exp(-rate[None] * (lags + 1.0)), axis=1
    )
    long_part = inner + carried
    long_part = long_part + skip_gain[None, :] * product
    mixed_local = (filtered[0] * long_part).astype(jnp.bfloat16)
    features = ring_gather(mixed_local, "tensor", 8)
    weight_all = lax.all_gather(out_weight, "seq", axis=0, tiled=True)
    ring = len(features)
    halves = features[0].shape[0]
    weight_all = weight_all.reshape(halves, ring, channels, weight_all.shape[1])
    place = lax.axis_index("tensor") % ring
    weight_all = jnp.roll(weight_all, -place, axis=1)
    projected = jnp.zeros((features[0].shape[1], weight_all.shape[-1]), jnp.float32)
    for r in range(ring):
        projected = projected + jnp.einsum(
            "htc,hco->to", features[r], weight_all[:, r], preferred_element_type=jnp.float32
        )
    return projected.astype(jnp.bfloat16)


def solution(mesh):
    return jax.shard_map(
        body,
        mesh=mesh,
        in_specs=(
            P(None, "seq", "tensor"),
            P(None, None, "tensor"),
            P(None, "tensor"),
            P(None, "tensor"),
            P("tensor"),
            P("seq", "tensor"),
        ),
        out_specs=P("seq", "tensor"),
        check_vma=False,
    )
```
